32 devices in a mesh: section: 4 (over y, x), ctx: 8 (over z, core).
Axes of the slice: x: 2, y: 2, z: 4, core: 2. Of those that a mesh axis runs over, the one named last changes fastest.
Arguments:
- queries: bfloat16 [4, 1024, 2048], P('section', 'ctx'), may hold values from -4.5 to 4.5
- keys_values: bfloat16 [4, 1024, 1024], P('section', 'ctx'), may hold values from -4.5 to 4.5
- mix_in: bfloat16 [4, 3, 1024, 4096], P('section', None, 'ctx'), may hold values from -11.5 to 4.5
- proj_bc: bfloat16 [4, 1024, 16], P('section', 'ctx'), may hold values from -12 to 12
- attn_cot: bfloat16 [4, 1024, 2048], P('section', 'ctx'), may hold values from -6 to 6
- mamba_cot: bfloat16 [4, 1024, 4096], P('section', 'ctx'), may hold values from -6 to 6
- conv_weight: float32 [4, 4, 4096], P('section'), may hold values from -3 to 3
- conv_bias: float32 [4, 4096], P('section'), may hold values from -3 to 3
- a_log: float32 [4, 8, 4096], P('section'), may hold values from -0.7 to 0.7
- skip_gain: float32 [4, 4096], P('section'), may hold values from 0.5 to 4
Outputs:
- attn_out: bfloat16 [4, 1024, 2048], P('section', 'ctx')
- mamba_out: bfloat16 [4, 1024, 4096], P('section', 'ctx')
- query_grads: bfloat16 [4, 1024, 2048], P('section', 'ctx')
- pair_grads: bfloat16 [4, 1024, 1024], P('section', 'ctx')
- mix_grads: bfloat16 [4, 3, 1024, 4096], P('section', None, 'ctx')
- bc_grads: bfloat16 [4, 1024, 16], P('section', 'ctx')
- conv_weight_grad: float32 [4, 4, 4096], P('section')
- conv_bias_grad: float32 [4, 4096], P('section')
- a_log_grad: float32 [4, 8, 4096], P('section')
- skip_grad: float32 [4, 4096], P('section')
The draws below stay inside these ranges and needn't reach their ends.
All inputs are finite; a program needn't handle non-finite values.
Results may differ from the reference program's by a relative error of at most 0.019.
Values may be sent and summed in bfloat16 or wider, within the bound.
No kernel may reach another device: no remote copies, remote signals or barrier semaphores. Data moves between devices by JAX's collectives and lax.ppermute only.
A program may use at most 256 MiB of HBM per device.

```python
import math
import jax
import jax.numpy as jnp
from jax import lax

TOK_DEV = 128
C = 4096
NSTATE = 8
KCONV = 4
HEADS = 16
KVHEADS = 4
HDIM = 128
SEQUENCE_TOKENS = 1024
RELAY_SECTIONS = 4
N_CTX = 8


def draw_queries(key, part):
    query_width = HEADS * HDIM
    base_draw = jnp.clip(2.5 * jax.random.normal(jax.random.fold_in(key, 2), (RELAY_SECTIONS, SEQUENCE_TOKENS, query_width), jnp.float32), -4.5, 4.5)
    return base_draw.astype(jnp.bfloat16)


def draw_keys_values(key, part):
    half_width = KVHEADS * HDIM
    base_draw = jnp.clip(jax.random.normal(jax.random.fold_in(key, 4), (RELAY_SECTIONS, SEQUENCE_TOKENS, 2 * half_width), jnp.float32), -4.5, 4.5)
    return base_draw.astype(jnp.bfloat16)


def draw_mix_in(key, part):
    signal = jax.random.normal(jax.random.fold_in(key, 11), (RELAY_SECTIONS, 2, SEQUENCE_TOKENS, C), jnp.float32)
    fast_share = 0.15
    middle_share = 0.35
    slow_low = -10.0
    slow_high = -9.3
    signal = jnp.clip(signal, -4.5, 4.5)
    class_pick = jax.random.uniform(jax.random.fold_in(key, 13), (RELAY_SECTIONS, 1, C), jnp.float32)
    fast_mask = class_pick < fast_share
    middle_mask = class_pick < fast_share + middle_share
    fast_level = jax.random.uniform(jax.random.fold_in(key, 14), (RELAY_SECTIONS, 1, C), jnp.float32, -4.0, -3.0)
    slow_level = jax.random.uniform(jax.random.fold_in(key, 15), (RELAY_SECTIONS, 1, C), jnp.float32, slow_low, slow_high)
    middle_level = jax.random.uniform(jax.random.fold_in(key, 19), (RELAY_SECTIONS, 1, C), jnp.float32, -7.4, -6.4)
    noise_levels = jnp.where(fast_mask, fast_level, jnp.where(middle_mask, middle_level, slow_level))
    section_offset = jax.random.uniform(jax.random.fold_in(key, 16), (RELAY_SECTIONS, SEQUENCE_TOKENS // TOK_DEV, 1), jnp.float32, -0.7, 0.7)
    section_offset = jnp.repeat(section_offset, TOK_DEV, axis=1)
    row_jitter = jax.random.uniform(jax.random.fold_in(key, 17), (RELAY_SECTIONS, SEQUENCE_TOKENS, C), jnp.float32, -0.5, 0.5)
    spike_rows = jax.random.randint(jax.random.fold_in(key, 18), (RELAY_SECTIONS, 6), 0, SEQUENCE_TOKENS)
    spike_events = jnp.any(jnp.arange(SEQUENCE_TOKENS)[None, :, None] == spike_rows[:, None, :], axis=2)[:, :, None]
    unscaled_step = jnp.where(spike_events, -1.05, noise_levels + section_offset + row_jitter)
    return jnp.concatenate([signal, unscaled_step[:, None]], axis=1).astype(jnp.bfloat16)


def block_levels(own_key, dims, split, smallest, top_value):
    factor_of = 1.0
    for dim, parts in split:
        heights = jax.random.uniform(jax.random.fold_in(jax.random.fold_in(own_key, 6), dim), (parts,), jnp.float32, smallest / len(split), top_value / len(split))
        factor_of = factor_of * jnp.repeat(jnp.exp(heights), dims[dim] // parts).reshape((-1,) + (1,) * (len(dims) - 1 - dim))
    return factor_of


def normal_values(stream_key, dims, deviation, most, shards=(), kind=jnp.bfloat16):
    array = jax.random.normal(stream_key, dims, jnp.float32) * deviation
    if len(shards) > 0:
        array = block_levels(stream_key, dims, shards, -0.22, 0.18) * array
    return jnp.clip(array, min=-most, max=most).astype(kind)


def setup_inputs(seed: int = 0) -> dict:
    seeds = jax.random.split(jax.random.key(seed), 11)
    queries = draw_queries(jax.random.fold_in(seeds[10], 71), 0)
    keys_values = draw_keys_values(jax.random.fold_in(seeds[10], 71), 0)
    mix_in = draw_mix_in(jax.random.fold_in(seeds[10], 71), 0)
    proj_bc = normal_values(seeds[3], (RELAY_SECTIONS, SEQUENCE_TOKENS, 2 * NSTATE), 3.0, 12.0, ((0, 4), (1, 8)))
    attn_cot = normal_values(seeds[4], (RELAY_SECTIONS, SEQUENCE_TOKENS, HEADS * HDIM), 1.0, 6.0, ((0, 4), (1, 8)))
    mamba_cot = normal_values(seeds[5], (RELAY_SECTIONS, SEQUENCE_TOKENS, C), 1.0, 6.0, ((0, 4), (1, 8)))
    conv_weight = normal_values(seeds[6], (RELAY_SECTIONS, KCONV, C), KCONV ** -0.5, 3.0, ((0, 4),), jnp.float32)
    conv_bias = normal_values(seeds[7], (RELAY_SECTIONS, C), 0.5, 3.0, ((0, 4),), jnp.float32)
    a_log = jnp.clip(jax.random.uniform(seeds[8], (RELAY_SECTIONS, NSTATE, C), jnp.float32, -0.7, 0.7) * block_levels(seeds[8], (RELAY_SECTIONS, NSTATE, C), ((0, 4),), -0.4, 0.0), -0.7, 0.7)
    skip_gain = jnp.clip(jnp.exp(math.log(4.0) - 2.0794415 * jax.random.uniform(seeds[9], (RELAY_SECTIONS, C), jnp.float32) ** block_levels(seeds[9], (RELAY_SECTIONS, C), ((0, 4),), -0.2, 0.2)), 0.5, 4.0)
    return dict(queries=queries, keys_values=keys_values, mix_in=mix_in, proj_bc=proj_bc, attn_cot=attn_cot, mamba_cot=mamba_cot, conv_weight=conv_weight, conv_bias=conv_bias, a_log=a_log, skip_gain=skip_gain)


def mamba_layer(mixture, projections, conv_taps, conv_shift, log_rates, direct_gain):
    signal = mixture[0]
    gating = mixture[1]
    unscaled_step = mixture[2]
    seq_length = signal.shape[0]
    padded = jnp.concatenate([jnp.zeros((KCONV - 1, signal.shape[1]), signal.dtype), signal], axis=0)
    preact = conv_shift
    for offset in range(KCONV):
        preact = preact + conv_taps[offset] * padded[offset:offset + seq_length]
    inner_act = jax.nn.silu(preact)
    step_size = jax.nn.softplus(unscaled_step)
    decay_rate = -jnp.exp(log_rates)
    b_proj = projections[:, :NSTATE]
    c_proj = projections[:, NSTATE:]

    def advance(state, row_in):
        step_row, b_row, c_row, inner_row = row_in
        state = jnp.exp(step_row[None, :] * decay_rate) * state + b_row[:, None] * (step_row * inner_row)[None, :]
        return (state, lax.optimization_barrier(jnp.sum(state * c_row[:, None], axis=0)))
    _, mixed_out = lax.scan(advance, jnp.zeros(decay_rate.shape, decay_rate.dtype), (step_size, b_proj, c_proj, inner_act))
    mixed_out = mixed_out + direct_gain * inner_act
    return mixed_out * jax.nn.silu(gating)

def attention_section(query_in, pair_in, attn_grad):
    seq_length = query_in.shape[0]
    group_size = HEADS // KVHEADS
    softmax_scale = HDIM ** (-0.5)
    query_heads = query_in.reshape(seq_length, KVHEADS, group_size, HDIM)
    grad_heads = attn_grad.reshape(seq_length, KVHEADS, group_size, HDIM)
    pair_rows = pair_in.reshape(seq_length, 2, KVHEADS, HDIM).astype(jnp.float32)
    key_rows = pair_rows[:, 0]
    value_rows = pair_rows[:, 1]
    key_pos = jnp.arange(seq_length).astype(jnp.int32)

    def per_block(running, block_index):
        first_row = (block_index * TOK_DEV).astype(jnp.int32)
        query_blk = lax.dynamic_slice_in_dim(query_heads, first_row, TOK_DEV, 0).astype(jnp.float32)
        grad_blk = lax.dynamic_slice_in_dim(grad_heads, first_row, TOK_DEV, 0).astype(jnp.float32)
        scores = jnp.einsum('tgrd,sgd->gtrs', query_blk, key_rows) * softmax_scale
        query_pos = first_row + jnp.arange(TOK_DEV).astype(jnp.int32)
        allowed = (key_pos[None, :] <= query_pos[:, None])[None, :, None, :]
        row_peak = lax.optimization_barrier(jnp.max(jnp.where(allowed, scores, -jnp.inf), axis=-1, keepdims=True))
        row_total = lax.optimization_barrier(jnp.sum(jnp.where(allowed, jnp.exp(scores - row_peak), 0.0), axis=-1, keepdims=True))
        probs_b = jnp.where(allowed, jnp.exp(scores - (row_peak + jnp.log(row_total))), 0.0).astype(jnp.bfloat16)
        probs_f = lax.optimization_barrier(probs_b).astype(jnp.float32)
        output = jnp.einsum('gtrs,sgd->tgrd', probs_f, value_rows).astype(jnp.bfloat16)
        prob_slope = jnp.einsum('tgrd,sgd->gtrs', grad_blk, value_rows)
        row_delta = jnp.einsum('tgrd,tgrd->gtr', grad_blk, output.astype(jnp.float32))[..., None]
        score_b = (probs_f * (prob_slope - row_delta)).astype(jnp.bfloat16)
        score_f = lax.optimization_barrier(score_b).astype(jnp.float32)
        query_grad = (jnp.einsum('gtrs,sgd->tgrd', score_f, key_rows) * softmax_scale).astype(jnp.bfloat16)
        key_term = jnp.einsum('gtrs,tgrd->sgd', score_f, query_blk) * softmax_scale
        value_term = jnp.einsum('gtrs,tgrd->sgd', probs_f, grad_blk)
        term_rows = lax.optimization_barrier(jnp.stack([key_term, value_term], axis=1).astype(jnp.bfloat16))
        return (running + term_rows.astype(jnp.float32), (output, query_grad))
    start_sum = jnp.zeros((seq_length, 2, KVHEADS, HDIM), jnp.float32)
    total_sum, (outputs, query_grads) = lax.scan(per_block, start_sum, jnp.arange(N_CTX).astype(jnp.int32))
    attn_out = outputs.reshape(seq_length, HEADS * HDIM)
    query_out = query_grads.reshape(seq_length, HEADS * HDIM)
    pair_out = total_sum.astype(jnp.bfloat16).reshape(seq_length, 2 * KVHEADS * HDIM)
    return (attn_out, query_out, pair_out)

def reference(queries, keys_values, mix_in, proj_bc, attn_cot, mamba_cot, conv_weight, conv_bias, a_log, skip_gain):
    collected = [[] for position in range(10)]
    for section_index in range(RELAY_SECTIONS):
        before_section = (section_index - 1) % RELAY_SECTIONS
        after_section = (section_index + 1) % RELAY_SECTIONS
        attn_out, query_out, pair_out = attention_section(queries[before_section], keys_values[before_section], attn_cot[after_section])
        mixture = mix_in[before_section].astype(jnp.float32)
        projections = proj_bc[before_section].astype(jnp.float32)
        mamba_full, pullback = jax.vjp(mamba_layer, mixture, projections, conv_weight[section_index], conv_bias[section_index], a_log[section_index], skip_gain[section_index])
        grad_list = pullback(mamba_cot[after_section].astype(jnp.float32))
        results = (attn_out, mamba_full.astype(jnp.bfloat16), query_out, pair_out, grad_list[0].astype(jnp.bfloat16), grad_list[1].astype(jnp.bfloat16), grad_list[2], grad_list[3], grad_list[4], grad_list[5])
        for position in range(10):
            collected[position].append(results[position])
    stacked = [jnp.stack(column, axis=0) for column in collected]
    return (stacked[0], stacked[1], stacked[2], stacked[3], stacked[4], stacked[5], stacked[6], stacked[7], stacked[8], stacked[9])
```

```python
import jax
import jax.numpy as jnp
from jax import lax
from jax.sharding import PartitionSpec as P
from jax.experimental import pallas as pl
from jax.experimental.pallas import tpu as pltpu

C = 4096
NSTATE = 8
KCONV = 4
HEADS = 16
KVHEADS = 4
HDIM = 128


def shifted(block, axis, distance):
    devices = range(lax.axis_size(axis))
    route = [((i - distance) % len(devices), i) for i in devices]
    return lax.ppermute(block, axis, route)


def passed_along(shard, axis, by):
    devices = lax.axis_size(axis)
    pairs = [(i, i + by) for i in range(devices) if 0 <= i + by < devices]
    return lax.ppermute(shard, axis, pairs)


def shortened(shard):

    def short(part):
        return part.astype(jnp.bfloat16) if part.dtype == jnp.float32 else part

    return jax.tree.map(short, shard)


def silu_slope(value):
    sigmoid_v = jax.nn.sigmoid(value)
    return sigmoid_v * (1.0 + value * (1.0 - sigmoid_v))


def attention_group(group_index, query_heads, grad_heads, key_whole, first_row, softmax_scale):
    query_g = lax.dynamic_index_in_dim(query_heads, group_index, 1, False)
    grad_g = lax.dynamic_index_in_dim(grad_heads, group_index, 1, False)
    pair_rows = lax.dynamic_index_in_dim(key_whole, group_index, 2, False)
    key_rows = pair_rows[:, 0]
    value_rows = pair_rows[:, 1]
    scores = (
        jnp.einsum("trd,sd->trs", query_g, key_rows, preferred_element_type=jnp.float32)
        * softmax_scale
    )
    query_pos = first_row + jnp.arange(query_g.shape[0], dtype=jnp.int32)
    key_pos = jnp.arange(key_rows.shape[0], dtype=jnp.int32)
    allowed = (key_pos[None, :] <= query_pos[:, None])[:, None, :]
    row_peak = jnp.max(jnp.where(allowed, scores, -jnp.inf), axis=-1, keepdims=True)
    row_total = jnp.sum(jnp.where(allowed, jnp.exp(scores - row_peak), 0.0), axis=-1, keepdims=True)
    probs_b = jnp.where(allowed, jnp.exp(scores - (row_peak + jnp.log(row_total))), 0.0).astype(
        jnp.bfloat16
    )
    output = jnp.einsum(
        "trs,sd->trd", probs_b, value_rows, preferred_element_type=jnp.float32
    ).astype(jnp.bfloat16)
    prob_slope = jnp.einsum("trd,sd->trs", grad_g, value_rows, preferred_element_type=jnp.float32)
    row_delta = jnp.sum(
        grad_g.astype(jnp.float32) * output.astype(jnp.float32), axis=-1, keepdims=True
    )
    score_grad = (probs_b.astype(jnp.float32) * (prob_slope - row_delta)).astype(jnp.bfloat16)
    query_grad = (
        jnp.einsum("trs,sd->trd", score_grad, key_rows, preferred_element_type=jnp.float32)
        * softmax_scale
    ).astype(jnp.bfloat16)
    return (output, query_grad, probs_b, score_grad)


def key_terms(probs_all, score_all, query_heads, grad_heads, softmax_scale):
    key_grad = (
        jnp.einsum("gtrs,tgrd->sgd", score_all, query_heads, preferred_element_type=jnp.float32)
        * softmax_scale
    )
    value_grad = jnp.einsum(
        "gtrs,tgrd->sgd", probs_all, grad_heads, preferred_element_type=jnp.float32
    )
    return jnp.stack([key_grad, value_grad], axis=1)


LANES = 128
ROWS = 8


def fold_rows(parts):
    rows = lax.broadcasted_iota(jnp.int32, parts[0].shape, 0)

    def pair(first, second, k):
        low = (rows & k) == 0
        kept = jnp.where(low, first, second)
        moved = jnp.where(low, second, first)
        if k == 4:
            swapped = pltpu.roll(moved, 4, 0)
        else:
            swapped = jnp.where(low, pltpu.roll(moved, ROWS - k, 0), pltpu.roll(moved, k, 0))
        return kept + swapped

    stage = [pair(parts[n], parts[n + 4], 4) for n in range(4)]
    stage = [pair(stage[n], stage[n + 2], 2) for n in range(2)]
    return pair(stage[0], stage[1], 1)


def summary_kernel(b_ref, c_ref, dt_ref, u_ref, gy_ref, a_ref, s_ref, g_ref):
    steps = dt_ref.shape[0]
    count = a_ref.shape[0]
    rates = [a_ref[n] for n in range(count)]

    def advance(t, carry):
        state, decay, adjoint = carry
        dt = dt_ref[t]
        moved = u_ref[t]
        drive = gy_ref[t]
        next_state, next_decay, next_adjoint = [], [], []
        for n in range(count):
            factor = jnp.exp(dt * rates[n])
            next_state.append(factor * state[n] + b_ref[t * count + n] * moved)
            d = decay[n] * factor
            next_decay.append(d)
            next_adjoint.append(adjoint[n] + (c_ref[t * count + n] * d) * drive)
        return (tuple(next_state), tuple(next_decay), tuple(next_adjoint))

    zeros = tuple(jnp.zeros_like(r) for r in rates)
    ones = tuple(jnp.ones_like(r) for r in rates)
    state, _, adjoint = lax.fori_loop(0, steps, advance, (zeros, ones, zeros), unroll=2)
    for n in range(count):
        s_ref[n] = state[n]
        g_ref[n] = adjoint[n]


def full_kernel(
    b_ref, c_ref, dt_ref, u_ref, gy_ref, a_ref, hin_ref, gin_ref,
    y_ref, gu_ref, gdt_ref, ga_ref, gc_ref, gb_ref, hist_ref,
):
    steps = dt_ref.shape[0]
    count = a_ref.shape[0]
    rates = [a_ref[n] for n in range(count)]
    start = tuple(hin_ref[n] for n in range(count))
    for n in range(count):
        hist_ref[0, n] = start[n]

    def forward(t, state):
        dt = dt_ref[t]
        moved = u_ref[t]
        drive = gy_ref[t]
        mixed = None
        parts = []
        next_state = []
        for n in range(count):
            factor = jnp.exp(dt * rates[n])
            h = factor * state[n] + b_ref[t * count + n] * moved
            hist_ref[t + 1, n] = h
            term = c_ref[t * count + n] * h
            mixed = term if mixed is None else mixed + term
            parts.append(h * drive)
            next_state.append(h)
        y_ref[t] = mixed
        gc_ref[t] = fold_rows(parts)
        return tuple(next_state)

    lax.fori_loop(0, steps, forward, start, unroll=2)

    def backward(i, carry):
        t = steps - 1 - i
        pending, rate_acc = carry
        dt = dt_ref[t]
        moved = u_ref[t]
        drive = gy_ref[t]
        step_acc = None
        moved_acc = None
        parts = []
        next_pending = []
        next_rate = []
        for n in range(count):
            factor = jnp.exp(dt * rates[n])
            adj = c_ref[t * count + n] * drive + pending[n]
            through = adj * factor * hist_ref[t, n]
            x1 = through * rates[n]
            step_acc = x1 if step_acc is None else step_acc + x1
            next_rate.append(rate_acc[n] + through * dt)
            x2 = b_ref[t * count + n] * adj
            moved_acc = x2 if moved_acc is None else moved_acc + x2
            parts.append(adj * moved)
            next_pending.append(factor * adj)
        gdt_ref[t] = step_acc
        gu_ref[t] = moved_acc
        gb_ref[t] = fold_rows(parts)
        return (tuple(next_pending), tuple(next_rate))

    pending0 = tuple(gin_ref[n] for n in range(count))
    zeros = tuple(jnp.zeros_like(r) for r in rates)
    _, rate_acc = lax.fori_loop(0, steps, backward, (pending0, zeros), unroll=2)
    for n in range(count):
        ga_ref[n] = rate_acc[n]


def scan_specs(steps, count, blocks):
    smem = pl.BlockSpec(memory_space=pltpu.SMEM)
    rows = pl.BlockSpec((steps, ROWS, LANES), lambda j: (0, j, 0))
    states = pl.BlockSpec((count, ROWS, LANES), lambda j: (0, j, 0))
    return smem, rows, states


def mamba_summary(b_flat, c_flat, dt_r, u_r, gy_r, a_r):
    steps = dt_r.shape[0]
    count = a_r.shape[0]
    blocks = dt_r.shape[1] // ROWS
    smem, rows, states = scan_specs(steps, count, blocks)
    shape = jax.ShapeDtypeStruct(a_r.shape, jnp.float32)
    elems = steps * count * dt_r.shape[1] * LANES
    return pl.pallas_call(
        summary_kernel,
        grid=(blocks,),
        in_specs=[smem, smem, rows, rows, rows, states],
        out_specs=[states, states],
        out_shape=[shape, shape],
        cost_estimate=pl.CostEstimate(
            flops=9 * elems, transcendentals=elems, bytes_accessed=4 * 3 * dt_r.size
        ),
    )(b_flat, c_flat, dt_r, u_r, gy_r, a_r)


def mamba_full(b_flat, c_flat, dt_r, u_r, gy_r, a_r, h_in, g_in):
    steps = dt_r.shape[0]
    count = a_r.shape[0]
    blocks = dt_r.shape[1] // ROWS
    smem, rows, states = scan_specs(steps, count, blocks)
    folded = pl.BlockSpec((None, steps, count, LANES), lambda j: (j, 0, 0, 0))
    row_shape = jax.ShapeDtypeStruct(dt_r.shape, jnp.float32)
    fold_shape = jax.ShapeDtypeStruct((blocks, steps, count, LANES), jnp.float32)
    elems = steps * count * dt_r.shape[1] * LANES
    return pl.pallas_call(
        full_kernel,
        grid=(blocks,),
        in_specs=[smem, smem, rows, rows, rows, states, states, states],
        out_specs=[rows, rows, rows, states, folded, folded],
        out_shape=[
            row_shape,
            row_shape,
            row_shape,
            jax.ShapeDtypeStruct(a_r.shape, jnp.float32),
            fold_shape,
            fold_shape,
        ],
        scratch_shapes=[pltpu.VMEM((steps + 1, count, ROWS, LANES), jnp.float32)],
        cost_estimate=pl.CostEstimate(
            flops=30 * elems, transcendentals=2 * elems, bytes_accessed=4 * 6 * dt_r.size
        ),
    )(b_flat, c_flat, dt_r, u_r, gy_r, a_r, h_in, g_in)


def lanes_view(matrix):
    return matrix.reshape(matrix.shape[0], matrix.shape[1] // LANES, LANES)


def flat_view(stacked):
    return stacked.reshape(stacked.shape[0], stacked.shape[1] * stacked.shape[2])


def body(
    queries,
    keys_values,
    mix_in,
    proj_bc,
    attn_cot,
    mamba_cot,
    conv_weight,
    conv_bias,
    a_log,
    skip_gain,
):
    query_in, pair_in, mixture, proj_in = shifted(
        (queries[0], keys_values[0], mix_in[0], proj_bc[0]), "section", 1
    )
    attn_grad, mamba_grad = shifted((attn_cot[0], mamba_cot[0]), "section", -1)
    row_count = query_in.shape[0]
    group_size = HEADS // KVHEADS
    softmax_scale = HDIM ** (-0.5)
    first_row = lax.axis_index("ctx") * row_count
    pairs_whole = lax.all_gather(pair_in, "ctx", axis=0, tiled=True)
    seq_length = pairs_whole.shape[0]
    key_whole = pairs_whole.reshape(seq_length, 2, KVHEADS, HDIM)
    query_heads = query_in.reshape(row_count, KVHEADS, group_size, HDIM)
    grad_heads = attn_grad.reshape(row_count, KVHEADS, group_size, HDIM)

    def per_group(group_index):
        return attention_group(
            group_index, query_heads, grad_heads, key_whole, first_row, softmax_scale
        )

    outputs, query_grads, probs_all, score_all = lax.map(
        per_group, jnp.arange(KVHEADS, dtype=jnp.int32)
    )
    attn_out = outputs.transpose(1, 0, 2, 3).reshape(row_count, HEADS * HDIM)
    query_out = query_grads.transpose(1, 0, 2, 3).reshape(row_count, HEADS * HDIM)
    whole_term = key_terms(probs_all, score_all, query_heads, grad_heads, softmax_scale)
    key_sum = lax.psum_scatter(
        whole_term.astype(jnp.bfloat16), "ctx", scatter_dimension=0, tiled=True
    )
    pair_out = key_sum.reshape(row_count, 2 * KVHEADS * HDIM)
    signal = mixture[0]
    gating = mixture[1]
    unscaled_step = mixture[2]
    conv_rows = KCONV - 1
    rim_rows = passed_along(signal[row_count - conv_rows :], "ctx", 1)
    padded = jnp.concatenate([rim_rows, signal], axis=0).astype(jnp.float32)
    conv_taps = conv_weight[0]
    preact = conv_bias[0]
    for offset in range(KCONV):
        preact = preact + conv_taps[offset] * padded[offset : offset + row_count]
    inner_act = jax.nn.silu(preact)
    step_size = jax.nn.softplus(unscaled_step.astype(jnp.float32))
    decay_rate = -jnp.exp(a_log[0])
    b_proj = proj_in[:, :NSTATE].astype(jnp.float32)
    c_proj = proj_in[:, NSTATE:].astype(jnp.float32)
    gating_f = gating.astype(jnp.float32)
    gate_act = jax.nn.silu(gating_f)
    out_grad = mamba_grad.astype(jnp.float32)
    out_drive = out_grad * gate_act
    moved_in = step_size * inner_act
    b_flat = b_proj.reshape(-1)
    c_flat = c_proj.reshape(-1)
    dt_r = lanes_view(step_size)
    u_r = lanes_view(moved_in)
    gy_r = lanes_view(out_drive)
    a_r = lanes_view(decay_rate)
    state_end, adjoint_end = mamba_summary(b_flat, c_flat, dt_r, u_r, gy_r, a_r)
    step_total = jnp.sum(dt_r, axis=0)
    gathered = lax.all_gather(
        jnp.concatenate([state_end, adjoint_end, step_total[None]], axis=0), "ctx"
    )
    count = a_r.shape[0]
    place = lax.axis_index("ctx")
    devices = gathered.shape[0]
    state_in = jnp.zeros_like(state_end)
    adjoint_in = jnp.zeros_like(adjoint_end)
    for other in range(devices):
        decay = jnp.exp(a_r * gathered[other, 2 * count][None])
        state_in = jnp.where(
            other < place, decay * state_in + gathered[other, :count], state_in
        )
    for other in reversed(range(devices)):
        decay = jnp.exp(a_r * gathered[other, 2 * count][None])
        adjoint_in = jnp.where(
            other > place, decay * adjoint_in + gathered[other, count : 2 * count], adjoint_in
        )
    y_ssm, moved_grad, step_ssm, rate_grad_r, c_fold, b_fold = mamba_full(
        b_flat, c_flat, dt_r, u_r, gy_r, a_r, state_in, adjoint_in
    )
    mixed_out = flat_view(y_ssm) + skip_gain[0] * inner_act
    step_grad = flat_view(step_ssm) + flat_view(moved_grad) * inner_act
    inner_grad = flat_view(moved_grad) * step_size + skip_gain[0] * out_drive
    rate_grad = flat_view(rate_grad_r)
    b_grad = jnp.sum(b_fold, axis=(0, 3))
    c_grad = jnp.sum(c_fold, axis=(0, 3))
    skip_grad = jnp.sum(out_drive * inner_act, axis=0)
    mamba_out = (mixed_out * gate_act).astype(jnp.bfloat16)
    gating_grad = out_grad * mixed_out * silu_slope(gating_f)
    raw_grad = step_grad * jax.nn.sigmoid(unscaled_step.astype(jnp.float32))
    pre_grad = inner_grad * silu_slope(preact)
    rim_after = passed_along(shortened(pre_grad[:conv_rows]), "ctx", -1)
    extended = jnp.concatenate([pre_grad, rim_after], axis=0)
    signal_grad = jnp.zeros_like(pre_grad)
    for offset in range(KCONV):
        signal_grad = (
            signal_grad
            + conv_taps[offset] * extended[conv_rows - offset : conv_rows - offset + row_count]
        )
    tap_grad = jnp.stack(
        [jnp.sum(pre_grad * padded[offset : offset + row_count], axis=0) for offset in range(KCONV)]
    )
    bias_grad = jnp.sum(pre_grad, axis=0)
    log_grad = rate_grad * decay_rate
    tap_sum, bias_sum, log_sum, skip_sum = (
        lax.psum(tap_grad.astype(jnp.bfloat16), "ctx").astype(jnp.float32),
        lax.psum(bias_grad.astype(jnp.bfloat16), "ctx").astype(jnp.float32),
        lax.psum(log_grad.astype(jnp.bfloat16), "ctx").astype(jnp.float32),
        lax.psum(skip_grad.astype(jnp.bfloat16), "ctx").astype(jnp.float32),
    )
    mix_out = jnp.stack([signal_grad, gating_grad, raw_grad]).astype(jnp.bfloat16)
    proj_out = jnp.concatenate([b_grad, c_grad], axis=1).astype(jnp.bfloat16)
    return (
        attn_out[None],
        mamba_out[None],
        query_out[None],
        pair_out[None],
        mix_out[None],
        proj_out[None],
        tap_sum[None],
        bias_sum[None],
        log_sum[None],
        skip_sum[None],
    )


def solution(mesh):
    placed = (
        P("section", "ctx", None),
        P("section", "ctx", None),
        P("section", None, "ctx", None),
        P("section", "ctx", None),
        P("section", "ctx", None),
        P("section", "ctx", None),
        P("section", None, None),
        P("section", None),
        P("section", None, None),
        P("section", None),
    )
    return jax.shard_map(
        body,
        mesh=mesh,
        in_specs=placed,
        out_specs=(
            P("section", "ctx", None),
            P("section", "ctx", None),
            P("section", "ctx", None),
            P("section", "ctx", None),
            P("section", None, "ctx", None),
            P("section", "ctx", None),
            P("section", None, None),
            P("section", None),
            P("section", None, None),
            P("section", None),
        ),
        check_vma=False,
    )
```

```python
import jax
import jax.numpy as jnp
from jax import lax
from jax.sharding import PartitionSpec as P
from jax.experimental import pallas as pl
from jax.experimental.pallas import tpu as pltpu

C = 4096
NSTATE = 8
KCONV = 4
HEADS = 16
KVHEADS = 4
HDIM = 128


def shifted(block, axis, distance):
    devices = range(lax.axis_size(axis))
    route = [((i - distance) % len(devices), i) for i in devices]
    return lax.ppermute(block, axis, route)


def passed_along(shard, axis, by):
    devices = lax.axis_size(axis)
    pairs = [(i, i + by) for i in range(devices) if 0 <= i + by < devices]
    return lax.ppermute(shard, axis, pairs)


def shortened(shard):

    def short(part):
        return part.astype(jnp.bfloat16) if part.dtype == jnp.float32 else part

    return jax.tree.map(short, shard)


def silu_slope(value):
    sigmoid_v = jax.nn.sigmoid(value)
    return sigmoid_v * (1.0 + value * (1.0 - sigmoid_v))


def attention_group(group_index, query_heads, grad_heads, key_whole, first_row, softmax_scale):
    query_g = lax.dynamic_index_in_dim(query_heads, group_index, 1, False)
    grad_g = lax.dynamic_index_in_dim(grad_heads, group_index, 1, False)
    pair_rows = lax.dynamic_index_in_dim(key_whole, group_index, 2, False)
    key_rows = pair_rows[:, 0]
    value_rows = pair_rows[:, 1]
    scores = (
        jnp.einsum("trd,sd->trs", query_g, key_rows, preferred_element_type=jnp.float32)
        * softmax_scale
    )
    query_pos = first_row + jnp.arange(query_g.shape[0], dtype=jnp.int32)
    key_pos = jnp.arange(key_rows.shape[0], dtype=jnp.int32)
    allowed = (key_pos[None, :] <= query_pos[:, None])[:, None, :]
    row_peak = jnp.max(jnp.where(allowed, scores, -jnp.inf), axis=-1, keepdims=True)
    row_total = jnp.sum(jnp.where(allowed, jnp.exp(scores - row_peak), 0.0), axis=-1, keepdims=True)
    probs_b = jnp.where(allowed, jnp.exp(scores - (row_peak + jnp.log(row_total))), 0.0).astype(
        jnp.bfloat16
    )
    output = jnp.einsum(
        "trs,sd->trd", probs_b, value_rows, preferred_element_type=jnp.float32
    ).astype(jnp.bfloat16)
    prob_slope = jnp.einsum("trd,sd->trs", grad_g, value_rows, preferred_element_type=jnp.float32)
    row_delta = jnp.sum(
        grad_g.astype(jnp.float32) * output.astype(jnp.float32), axis=-1, keepdims=True
    )
    score_grad = (probs_b.astype(jnp.float32) * (prob_slope - row_delta)).astype(jnp.bfloat16)
    query_grad = (
        jnp.einsum("trs,sd->trd", score_grad, key_rows, preferred_element_type=jnp.float32)
        * softmax_scale
    ).astype(jnp.bfloat16)
    return (output, query_grad, probs_b, score_grad)


def key_terms(probs_all, score_all, query_heads, grad_heads, softmax_scale):
    key_grad = (
        jnp.einsum("gtrs,tgrd->sgd", score_all, query_heads, preferred_element_type=jnp.float32)
        * softmax_scale
    )
    value_grad = jnp.einsum(
        "gtrs,tgrd->sgd", probs_all, grad_heads, preferred_element_type=jnp.float32
    )
    return jnp.stack([key_grad, value_grad], axis=1)


LANES = 128
ROWS = 8


def fold_rows(parts):
    rows = lax.broadcasted_iota(jnp.int32, parts[0].shape, 0)

    def pair(first, second, k):
        low = (rows & k) == 0
        kept = jnp.where(low, first, second)
        moved = jnp.where(low, second, first)
        if k == 4:
            swapped = pltpu.roll(moved, 4, 0)
        else:
            swapped = jnp.where(low, pltpu.roll(moved, ROWS - k, 0), pltpu.roll(moved, k, 0))
        return kept + swapped

    stage = [pair(parts[n], parts[n + 4], 4) for n in range(4)]
    stage = [pair(stage[n], stage[n + 2], 2) for n in range(2)]
    return pair(stage[0], stage[1], 1)


def summary_kernel(b_ref, c_ref, dt_ref, u_ref, gy_ref, a_ref, s_ref, g_ref):
    steps = dt_ref.shape[0]
    count = a_ref.shape[0]
    rates = [a_ref[n] for n in range(count)]

    def advance(t, carry):
        state, decay, adjoint = carry
        dt = dt_ref[t]
        moved = u_ref[t]
        drive = gy_ref[t]
        next_state, next_decay, next_adjoint = [], [], []
        for n in range(count):
            factor = jnp.exp(dt * rates[n])
            next_state.append(factor * state[n] + b_ref[t * count + n] * moved)
            d = decay[n] * factor
            next_decay.append(d)
            next_adjoint.append(adjoint[n] + (c_ref[t * count + n] * d) * drive)
        return (tuple(next_state), tuple(next_decay), tuple(next_adjoint))

    zeros = tuple(jnp.zeros_like(r) for r in rates)
    ones = tuple(jnp.ones_like(r) for r in rates)
    state, _, adjoint = lax.fori_loop(0, steps, advance, (zeros, ones, zeros), unroll=2)
    for n in range(count):
        s_ref[n] = state[n]
        g_ref[n] = adjoint[n]


def full_kernel(
    b_ref, c_ref, dt_ref, u_ref, gy_ref, a_ref, hin_ref, gin_ref,
    y_ref, gu_ref, gdt_ref, ga_ref, gc_ref, gb_ref, hist_ref,
):
    steps = dt_ref.shape[0]
    count = a_ref.shape[0]
    rates = [a_ref[n] for n in range(count)]
    start = tuple(hin_ref[n] for n in range(count))
    for n in range(count):
        hist_ref[0, n] = start[n]

    def forward(t, state):
        dt = dt_ref[t]
        moved = u_ref[t]
        drive = gy_ref[t]
        mixed = None
        parts = []
        next_state = []
        for n in range(count):
            factor = jnp.exp(dt * rates[n])
            h = factor * state[n] + b_ref[t * count + n] * moved
            hist_ref[t + 1, n] = h
            term = c_ref[t * count + n] * h
            mixed = term if mixed is None else mixed + term
            parts.append(h * drive)
            next_state.append(h)
        y_ref[t] = mixed
        gc_ref[t] = fold_rows(parts)
        return tuple(next_state)

    lax.fori_loop(0, steps, forward, start, unroll=2)

    def backward(i, carry):
        t = steps - 1 - i
        pending, rate_acc = carry
        dt = dt_ref[t]
        moved = u_ref[t]
        drive = gy_ref[t]
        step_acc = None
        moved_acc = None
        parts = []
        next_pending = []
        next_rate = []
        for n in range(count):
            factor = jnp.exp(dt * rates[n])
            adj = c_ref[t * count + n] * drive + pending[n]
            through = adj * factor * hist_ref[t, n]
            x1 = through * rates[n]
            step_acc = x1 if step_acc is None else step_acc + x1
            next_rate.append(rate_acc[n] + through * dt)
            x2 = b_ref[t * count + n] * adj
            moved_acc = x2 if moved_acc is None else moved_acc + x2
            parts.append(adj * moved)
            next_pending.append(factor * adj)
        gdt_ref[t] = step_acc
        gu_ref[t] = moved_acc
        gb_ref[t] = fold_rows(parts)
        return (tuple(next_pending), tuple(next_rate))

    pending0 = tuple(gin_ref[n] for n in range(count))
    zeros = tuple(jnp.zeros_like(r) for r in rates)
    _, rate_acc = lax.fori_loop(0, steps, backward, (pending0, zeros), unroll=2)
    for n in range(count):
        ga_ref[n] = rate_acc[n]


def scan_specs(steps, count, blocks):
    smem = pl.BlockSpec(memory_space=pltpu.SMEM)
    rows = pl.BlockSpec((steps, ROWS, LANES), lambda j: (0, j, 0))
    states = pl.BlockSpec((count, ROWS, LANES), lambda j: (0, j, 0))
    return smem, rows, states


def mamba_summary(b_flat, c_flat, dt_r, u_r, gy_r, a_r):
    steps = dt_r.shape[0]
    count = a_r.shape[0]
    blocks = dt_r.shape[1] // ROWS
    smem, rows, states = scan_specs(steps, count, blocks)
    shape = jax.ShapeDtypeStruct(a_r.shape, jnp.float32)
    elems = steps * count * dt_r.shape[1] * LANES
    return pl.pallas_call(
        summary_kernel,
        grid=(blocks,),
        in_specs=[smem, smem, rows, rows, rows, states],
        out_specs=[states, states],
        out_shape=[shape, shape],
        cost_estimate=pl.CostEstimate(
            flops=9 * elems, transcendentals=elems, bytes_accessed=4 * 3 * dt_r.size
        ),
    )(b_flat, c_flat, dt_r, u_r, gy_r, a_r)


def mamba_full(b_flat, c_flat, dt_r, u_r, gy_r, a_r, h_in, g_in):
    steps = dt_r.shape[0]
    count = a_r.shape[0]
    blocks = dt_r.shape[1] // ROWS
    smem, rows, states = scan_specs(steps, count, blocks)
    folded = pl.BlockSpec((None, steps, count, LANES), lambda j: (j, 0, 0, 0))
    row_shape = jax.ShapeDtypeStruct(dt_r.shape, jnp.float32)
    fold_shape = jax.ShapeDtypeStruct((blocks, steps, count, LANES), jnp.float32)
    elems = steps * count * dt_r.shape[1] * LANES
    return pl.pallas_call(
        full_kernel,
        grid=(blocks,),
        in_specs=[smem, smem, rows, rows, rows, states, states, states],
        out_specs=[rows, rows, rows, states, folded, folded],
        out_shape=[
            row_shape,
            row_shape,
            row_shape,
            jax.ShapeDtypeStruct(a_r.shape, jnp.float32),
            fold_shape,
            fold_shape,
        ],
        scratch_shapes=[pltpu.VMEM((steps + 1, count, ROWS, LANES), jnp.float32)],
        cost_estimate=pl.CostEstimate(
            flops=30 * elems, transcendentals=2 * elems, bytes_accessed=4 * 6 * dt_r.size
        ),
    )(b_flat, c_flat, dt_r, u_r, gy_r, a_r, h_in, g_in)


def lanes_view(matrix):
    return matrix.reshape(matrix.shape[0], matrix.shape[1] // LANES, LANES)


def flat_view(stacked):
    return stacked.reshape(stacked.shape[0], stacked.shape[1] * stacked.shape[2])


def mamba_chunk(mixture, mamba_grad, proj_in, conv_taps, conv_shift, log_rates, direct_gain):
    signal = mixture[0]
    gating = mixture[1]
    unscaled_step = mixture[2]
    row_count = signal.shape[0]
    conv_rows = KCONV - 1
    rim_rows = passed_along(signal[row_count - conv_rows :], "ctx", 1)
    padded = jnp.concatenate([rim_rows, signal], axis=0).astype(jnp.float32)
    preact = conv_shift
    for offset in range(KCONV):
        preact = preact + conv_taps[offset] * padded[offset : offset + row_count]
    inner_act = jax.nn.silu(preact)
    step_size = jax.nn.softplus(unscaled_step.astype(jnp.float32))
    decay_rate = -jnp.exp(log_rates)
    b_proj = proj_in[:, :NSTATE].astype(jnp.float32)
    c_proj = proj_in[:, NSTATE:].astype(jnp.float32)
    gating_f = gating.astype(jnp.float32)
    gate_act = jax.nn.silu(gating_f)
    out_grad = mamba_grad.astype(jnp.float32)
    out_drive = out_grad * gate_act
    moved_in = step_size * inner_act
    b_flat = b_proj.reshape(-1)
    c_flat = c_proj.reshape(-1)
    dt_r = lanes_view(step_size)
    u_r = lanes_view(moved_in)
    gy_r = lanes_view(out_drive)
    a_r = lanes_view(decay_rate)
    state_end, adjoint_end = mamba_summary(b_flat, c_flat, dt_r, u_r, gy_r, a_r)
    step_total = jnp.sum(dt_r, axis=0)
    gathered = lax.all_gather(
        jnp.concatenate([state_end, adjoint_end, step_total[None]], axis=0), "ctx"
    )
    count = a_r.shape[0]
    place = lax.axis_index("ctx")
    devices = gathered.shape[0]
    state_in = jnp.zeros_like(state_end)
    adjoint_in = jnp.zeros_like(adjoint_end)
    for other in range(devices):
        decay = jnp.exp(a_r * gathered[other, 2 * count][None])
        state_in = jnp.where(
            other < place, decay * state_in + gathered[other, :count], state_in
        )
    for other in reversed(range(devices)):
        decay = jnp.exp(a_r * gathered[other, 2 * count][None])
        adjoint_in = jnp.where(
            other > place, decay * adjoint_in + gathered[other, count : 2 * count], adjoint_in
        )
    y_ssm, moved_grad, step_ssm, rate_grad_r, c_fold, b_fold = mamba_full(
        b_flat, c_flat, dt_r, u_r, gy_r, a_r, state_in, adjoint_in
    )
    mixed_out = flat_view(y_ssm) + direct_gain * inner_act
    step_grad = flat_view(step_ssm) + flat_view(moved_grad) * inner_act
    inner_grad = flat_view(moved_grad) * step_size + direct_gain * out_drive
    rate_grad = flat_view(rate_grad_r)
    b_grad = jnp.sum(b_fold, axis=(0, 3))
    c_grad = jnp.sum(c_fold, axis=(0, 3))
    skip_grad = jnp.sum(out_drive * inner_act, axis=0)
    mamba_out = (mixed_out * gate_act).astype(jnp.bfloat16)
    gating_grad = out_grad * mixed_out * silu_slope(gating_f)
    raw_grad = step_grad * jax.nn.sigmoid(unscaled_step.astype(jnp.float32))
    pre_grad = inner_grad * silu_slope(preact)
    rim_after = passed_along(shortened(pre_grad[:conv_rows]), "ctx", -1)
    extended = jnp.concatenate([pre_grad, rim_after], axis=0)
    signal_grad = jnp.zeros_like(pre_grad)
    for offset in range(KCONV):
        signal_grad = (
            signal_grad
            + conv_taps[offset] * extended[conv_rows - offset : conv_rows - offset + row_count]
        )
    tap_grad = jnp.stack(
        [jnp.sum(pre_grad * padded[offset : offset + row_count], axis=0) for offset in range(KCONV)]
    )
    bias_grad = jnp.sum(pre_grad, axis=0)
    log_grad = rate_grad * decay_rate
    weight_parts = jnp.concatenate(
        [tap_grad, bias_grad[None], log_grad, skip_grad[None]], axis=0
    ).astype(jnp.bfloat16)
    mix_out = jnp.stack([signal_grad, gating_grad, raw_grad]).astype(jnp.bfloat16)
    return mamba_out, mix_out, b_grad, c_grad, weight_parts


def body(
    queries,
    keys_values,
    mix_in,
    proj_bc,
    attn_cot,
    mamba_cot,
    conv_weight,
    conv_bias,
    a_log,
    skip_gain,
):
    query_in, pair_in, proj_in = shifted((queries[0], keys_values[0], proj_bc[0]), "section", 1)
    attn_grad = shifted(attn_cot[0], "section", -1)
    mix_local, cot_local, _, _, _ = lax.optimization_barrier(
        (mix_in[0], mamba_cot[0], query_in, pair_in, attn_grad)
    )
    channels = mix_local.shape[-1]
    pieces = 2 if channels % (2 * ROWS * LANES) == 0 else 1
    width = channels // pieces
    arrived = []
    for piece in range(pieces):
        mix_part = mix_local[:, :, piece * width : (piece + 1) * width]
        cot_part = cot_local[:, piece * width : (piece + 1) * width]
        if arrived:
            mix_part, cot_part, _, _ = lax.optimization_barrier(
                (mix_part, cot_part) + arrived[-1]
            )
        arrived.append((shifted(mix_part, "section", 1), shifted(cot_part, "section", -1)))
    row_count = query_in.shape[0]
    group_size = HEADS // KVHEADS
    softmax_scale = HDIM ** (-0.5)
    first_row = lax.axis_index("ctx") * row_count
    pairs_whole = lax.all_gather(pair_in, "ctx", axis=0, tiled=True)
    seq_length = pairs_whole.shape[0]
    key_whole = pairs_whole.reshape(seq_length, 2, KVHEADS, HDIM)
    query_heads = query_in.reshape(row_count, KVHEADS, group_size, HDIM)
    grad_heads = attn_grad.reshape(row_count, KVHEADS, group_size, HDIM)

    def per_group(group_index):
        return attention_group(
            group_index, query_heads, grad_heads, key_whole, first_row, softmax_scale
        )

    outputs, query_grads, probs_all, score_all = lax.map(
        per_group, jnp.arange(KVHEADS, dtype=jnp.int32)
    )
    attn_out = outputs.transpose(1, 0, 2, 3).reshape(row_count, HEADS * HDIM)
    query_out = query_grads.transpose(1, 0, 2, 3).reshape(row_count, HEADS * HDIM)
    whole_term = key_terms(probs_all, score_all, query_heads, grad_heads, softmax_scale)
    first_mix, first_cot, attn_out, query_out, whole_term = lax.optimization_barrier(
        arrived[0] + (attn_out, query_out, whole_term)
    )
    arrived[0] = (first_mix, first_cot)
    key_sum = lax.psum_scatter(
        whole_term.astype(jnp.bfloat16), "ctx", scatter_dimension=0, tiled=True
    )
    pair_out = key_sum.reshape(row_count, 2 * KVHEADS * HDIM)
    results = []
    for piece, (mix_part, cot_part) in enumerate(arrived):
        cut = slice(piece * width, (piece + 1) * width)
        results.append(
            mamba_chunk(
                mix_part,
                cot_part,
                proj_in,
                conv_weight[0][:, cut],
                conv_bias[0][cut],
                a_log[0][:, cut],
                skip_gain[0][cut],
            )
        )
    mamba_out = jnp.concatenate([r[0] for r in results], axis=1)
    mix_out = jnp.concatenate([r[1] for r in results], axis=2)
    b_grad = sum(r[2] for r in results)
    c_grad = sum(r[3] for r in results)
    weight_parts = jnp.concatenate([r[4] for r in results], axis=1)
    weight_sum = jnp.sum(lax.all_gather(weight_parts, "ctx").astype(jnp.float32), axis=0)
    taps = conv_weight.shape[1]
    states = a_log.shape[1]
    tap_sum = weight_sum[:taps]
    bias_sum = weight_sum[taps]
    log_sum = weight_sum[taps + 1 : taps + 1 + states]
    skip_sum = weight_sum[taps + 1 + states]
    proj_out = jnp.concatenate([b_grad, c_grad], axis=1).astype(jnp.bfloat16)
    return (
        attn_out[None],
        mamba_out[None],
        query_out[None],
        pair_out[None],
        mix_out[None],
        proj_out[None],
        tap_sum[None],
        bias_sum[None],
        log_sum[None],
        skip_sum[None],
    )


def solution(mesh):
    placed = (
        P("section", "ctx", None),
        P("section", "ctx", None),
        P("section", None, "ctx", None),
        P("section", "ctx", None),
        P("section", "ctx", None),
        P("section", "ctx", None),
        P("section", None, None),
        P("section", None),
        P("section", None, None),
        P("section", None),
    )
    return jax.shard_map(
        body,
        mesh=mesh,
        in_specs=placed,
        out_specs=(
            P("section", "ctx", None),
            P("section", "ctx", None),
            P("section", "ctx", None),
            P("section", "ctx", None),
            P("section", None, "ctx", None),
            P("section", "ctx", None),
            P("section", None, None),
            P("section", None),
            P("section", None, None),
            P("section", None),
        ),
        check_vma=False,
    )
```

```python
import jax
import jax.numpy as jnp
from jax import lax
from jax.sharding import PartitionSpec as P
from jax.experimental import pallas as pl
from jax.experimental.pallas import tpu as pltpu

C = 4096
NSTATE = 8
KCONV = 4
HEADS = 16
KVHEADS = 4
HDIM = 128


def shifted(block, axis, distance):
    devices = range(lax.axis_size(axis))
    route = [((i - distance) % len(devices), i) for i in devices]
    return lax.ppermute(block, axis, route)


def passed_along(shard, axis, by):
    devices = lax.axis_size(axis)
    pairs = [(i, i + by) for i in range(devices) if 0 <= i + by < devices]
    return lax.ppermute(shard, axis, pairs)


def shortened(shard):

    def short(part):
        return part.astype(jnp.bfloat16) if part.dtype == jnp.float32 else part

    return jax.tree.map(short, shard)


def silu_slope(value):
    sigmoid_v = jax.nn.sigmoid(value)
    return sigmoid_v * (1.0 + value * (1.0 - sigmoid_v))


def attention_kernel(row_ref, q_ref, kv_ref, g_ref, o_ref, dq_ref, dkv_ref):
    rows = q_ref.shape[0]
    seq = kv_ref.shape[0]
    width = HDIM
    groups = kv_ref.shape[1] // (2 * width)
    heads = q_ref.shape[1] // width // groups
    scale = width ** (-0.5)
    query_pos = row_ref[0] + lax.broadcasted_iota(jnp.int32, (rows, seq), 0)
    key_pos = lax.broadcasted_iota(jnp.int32, (rows, seq), 1)
    allowed = key_pos <= query_pos

    def group(g, carry):
        key_col = pl.multiple_of(g * width, width)
        value_col = pl.multiple_of((groups + g) * width, width)
        keys = kv_ref[:, pl.ds(key_col, width)]
        values = kv_ref[:, pl.ds(value_col, width)]
        key_acc = jnp.zeros((seq, width), jnp.float32)
        value_acc = jnp.zeros((seq, width), jnp.float32)
        for r in range(heads):
            col = pl.multiple_of((g * heads + r) * width, width)
            cols = pl.ds(col, width)
            query = q_ref[:, cols]
            grad = g_ref[:, cols]
            scores = lax.dot_general(
                query, keys, (((1,), (1,)), ((), ())), preferred_element_type=jnp.float32
            ) * scale
            masked = jnp.where(allowed, scores, -jnp.inf)
            peak = jnp.max(masked, axis=-1, keepdims=True)
            total = jnp.sum(jnp.exp(masked - peak), axis=-1, keepdims=True)
            probs = jnp.exp(masked - (peak + jnp.log(total))).astype(jnp.bfloat16)
            output = jnp.dot(probs, values, preferred_element_type=jnp.float32).astype(
                jnp.bfloat16
            )
            o_ref[:, cols] = output
            slope = lax.dot_general(
                grad, values, (((1,), (1,)), ((), ())), preferred_element_type=jnp.float32
            )
            delta = jnp.sum(
                grad.astype(jnp.float32) * output.astype(jnp.float32), axis=-1, keepdims=True
            )
            score_grad = (probs.astype(jnp.float32) * (slope - delta)).astype(jnp.bfloat16)
            dq_ref[:, cols] = (
                jnp.dot(score_grad, keys, preferred_element_type=jnp.float32) * scale
            ).astype(jnp.bfloat16)
            key_acc = key_acc + lax.dot_general(
                score_grad, query, (((0,), (0,)), ((), ())), preferred_element_type=jnp.float32
            )
            value_acc = value_acc + lax.dot_general(
                probs, grad, (((0,), (0,)), ((), ())), preferred_element_type=jnp.float32
            )
        dkv_ref[:, pl.ds(key_col, width)] = (key_acc * scale).astype(jnp.bfloat16)
        dkv_ref[:, pl.ds(value_col, width)] = value_acc.astype(jnp.bfloat16)
        return carry

    lax.fori_loop(0, groups, group, 0)


def attention(first_row, query_in, pairs_whole, attn_grad):
    rows = query_in.shape[0]
    seq = pairs_whole.shape[0]
    smem = pl.BlockSpec(memory_space=pltpu.SMEM)
    whole = pl.BlockSpec(memory_space=pltpu.VMEM)
    flops = 12 * rows * seq * query_in.shape[1]
    return pl.pallas_call(
        attention_kernel,
        in_specs=[smem, whole, whole, whole],
        out_specs=[whole, whole, whole],
        out_shape=[
            jax.ShapeDtypeStruct(query_in.shape, jnp.bfloat16),
            jax.ShapeDtypeStruct(query_in.shape, jnp.bfloat16),
            jax.ShapeDtypeStruct(pairs_whole.shape, jnp.bfloat16),
        ],
        cost_estimate=pl.CostEstimate(
            flops=flops,
            transcendentals=2 * rows * seq * query_in.shape[1] // HDIM,
            bytes_accessed=2 * (4 * query_in.size + 2 * pairs_whole.size),
        ),
    )(first_row.reshape(1), query_in, pairs_whole, attn_grad)


LANES = 128
ROWS = 8


def fold_rows(parts):
    rows = lax.broadcasted_iota(jnp.int32, parts[0].shape, 0)

    def pair(first, second, k):
        low = (rows & k) == 0
        kept = jnp.where(low, first, second)
        moved = jnp.where(low, second, first)
        if k == 4:
            swapped = pltpu.roll(moved, 4, 0)
        else:
            swapped = jnp.where(low, pltpu.roll(moved, ROWS - k, 0), pltpu.roll(moved, k, 0))
        return kept + swapped

    stage = [pair(parts[n], parts[n + 4], 4) for n in range(4)]
    stage = [pair(stage[n], stage[n + 2], 2) for n in range(2)]
    return pair(stage[0], stage[1], 1)


def summary_kernel(b_ref, c_ref, dt_ref, u_ref, gy_ref, a_ref, s_ref, g_ref):
    steps = dt_ref.shape[0]
    count = a_ref.shape[0]
    rates = [a_ref[n] for n in range(count)]

    def advance(t, carry):
        state, decay, adjoint = carry
        dt = dt_ref[t]
        moved = u_ref[t]
        drive = gy_ref[t]
        next_state, next_decay, next_adjoint = [], [], []
        for n in range(count):
            factor = jnp.exp(dt * rates[n])
            next_state.append(factor * state[n] + b_ref[t * count + n] * moved)
            d = decay[n] * factor
            next_decay.append(d)
            next_adjoint.append(adjoint[n] + (c_ref[t * count + n] * d) * drive)
        return (tuple(next_state), tuple(next_decay), tuple(next_adjoint))

    zeros = tuple(jnp.zeros_like(r) for r in rates)
    ones = tuple(jnp.ones_like(r) for r in rates)
    state, _, adjoint = lax.fori_loop(0, steps, advance, (zeros, ones, zeros), unroll=2)
    for n in range(count):
        s_ref[n] = state[n]
        g_ref[n] = adjoint[n]


def full_kernel(
    b_ref, c_ref, dt_ref, u_ref, gy_ref, a_ref, hin_ref, gin_ref,
    y_ref, gu_ref, gdt_ref, ga_ref, gc_ref, gb_ref, hist_ref,
):
    steps = dt_ref.shape[0]
    count = a_ref.shape[0]
    rates = [a_ref[n] for n in range(count)]
    start = tuple(hin_ref[n] for n in range(count))
    for n in range(count):
        hist_ref[0, n] = start[n]

    def forward(t, state):
        dt = dt_ref[t]
        moved = u_ref[t]
        drive = gy_ref[t]
        mixed = None
        parts = []
        next_state = []
        for n in range(count):
            factor = jnp.exp(dt * rates[n])
            h = factor * state[n] + b_ref[t * count + n] * moved
            hist_ref[t + 1, n] = h
            term = c_ref[t * count + n] * h
            mixed = term if mixed is None else mixed + term
            parts.append(h * drive)
            next_state.append(h)
        y_ref[t] = mixed
        gc_ref[t] = fold_rows(parts)
        return tuple(next_state)

    lax.fori_loop(0, steps, forward, start, unroll=2)

    def backward(i, carry):
        t = steps - 1 - i
        pending, rate_acc = carry
        dt = dt_ref[t]
        moved = u_ref[t]
        drive = gy_ref[t]
        step_acc = None
        moved_acc = None
        parts = []
        next_pending = []
        next_rate = []
        for n in range(count):
            factor = jnp.exp(dt * rates[n])
            adj = c_ref[t * count + n] * drive + pending[n]
            through = adj * factor * hist_ref[t, n]
            x1 = through * rates[n]
            step_acc = x1 if step_acc is None else step_acc + x1
            next_rate.append(rate_acc[n] + through * dt)
            x2 = b_ref[t * count + n] * adj
            moved_acc = x2 if moved_acc is None else moved_acc + x2
            parts.append(adj * moved)
            next_pending.append(factor * adj)
        gdt_ref[t] = step_acc
        gu_ref[t] = moved_acc
        gb_ref[t] = fold_rows(parts)
        return (tuple(next_pending), tuple(next_rate))

    pending0 = tuple(gin_ref[n] for n in range(count))
    zeros = tuple(jnp.zeros_like(r) for r in rates)
    _, rate_acc = lax.fori_loop(0, steps, backward, (pending0, zeros), unroll=2)
    for n in range(count):
        ga_ref[n] = rate_acc[n]


def scan_specs(steps, count, blocks):
    smem = pl.BlockSpec(memory_space=pltpu.SMEM)
    rows = pl.BlockSpec((steps, ROWS, LANES), lambda j: (0, j, 0))
    states = pl.BlockSpec((count, ROWS, LANES), lambda j: (0, j, 0))
    return smem, rows, states


def mamba_summary(b_flat, c_flat, dt_r, u_r, gy_r, a_r):
    steps = dt_r.shape[0]
    count = a_r.shape[0]
    blocks = dt_r.shape[1] // ROWS
    smem, rows, states = scan_specs(steps, count, blocks)
    shape = jax.ShapeDtypeStruct(a_r.shape, jnp.float32)
    elems = steps * count * dt_r.shape[1] * LANES
    return pl.pallas_call(
        summary_kernel,
        grid=(blocks,),
        in_specs=[smem, smem, rows, rows, rows, states],
        out_specs=[states, states],
        out_shape=[shape, shape],
        cost_estimate=pl.CostEstimate(
            flops=9 * elems, transcendentals=elems, bytes_accessed=4 * 3 * dt_r.size
        ),
    )(b_flat, c_flat, dt_r, u_r, gy_r, a_r)


def mamba_full(b_flat, c_flat, dt_r, u_r, gy_r, a_r, h_in, g_in):
    steps = dt_r.shape[0]
    count = a_r.shape[0]
    blocks = dt_r.shape[1] // ROWS
    smem, rows, states = scan_specs(steps, count, blocks)
    folded = pl.BlockSpec((None, steps, count, LANES), lambda j: (j, 0, 0, 0))
    row_shape = jax.ShapeDtypeStruct(dt_r.shape, jnp.float32)
    fold_shape = jax.ShapeDtypeStruct((blocks, steps, count, LANES), jnp.float32)
    elems = steps * count * dt_r.shape[1] * LANES
    return pl.pallas_call(
        full_kernel,
        grid=(blocks,),
        in_specs=[smem, smem, rows, rows, rows, states, states, states],
        out_specs=[rows, rows, rows, states, folded, folded],
        out_shape=[
            row_shape,
            row_shape,
            row_shape,
            jax.ShapeDtypeStruct(a_r.shape, jnp.float32),
            fold_shape,
            fold_shape,
        ],
        scratch_shapes=[pltpu.VMEM((steps + 1, count, ROWS, LANES), jnp.float32)],
        cost_estimate=pl.CostEstimate(
            flops=30 * elems, transcendentals=2 * elems, bytes_accessed=4 * 6 * dt_r.size
        ),
    )(b_flat, c_flat, dt_r, u_r, gy_r, a_r, h_in, g_in)


def lanes_view(matrix):
    return matrix.reshape(matrix.shape[0], matrix.shape[1] // LANES, LANES)


def flat_view(stacked):
    return stacked.reshape(stacked.shape[0], stacked.shape[1] * stacked.shape[2])


def ctx_scan(decay_sum, carried, rates, axis, backward):
    count = lax.axis_size(axis)
    step = -1 if backward else 1
    merged = passed_along(jnp.concatenate([decay_sum, carried], axis=0), axis, step)
    distance = 1
    while distance < count:
        other = passed_along(merged, axis, step * distance)
        own_sum = merged[:1]
        merged = jnp.concatenate(
            [own_sum + other[:1], jnp.exp(rates * own_sum) * other[1:] + merged[1:]], axis=0
        )
        distance *= 2
    return merged[1:]


def ctx_total(parts, axis):
    count = lax.axis_size(axis)
    if count & (count - 1):
        return jnp.sum(lax.all_gather(parts, axis), axis=0)
    distance = 1
    while distance < count:
        pairs = [(i, i ^ distance) for i in range(count)]
        parts = parts + lax.ppermute(parts, axis, pairs)
        distance *= 2
    return parts


def mamba_chunk(mixture, mamba_grad, proj_in, conv_taps, conv_shift, log_rates, direct_gain):
    signal = mixture[0]
    gating = mixture[1]
    unscaled_step = mixture[2]
    row_count = signal.shape[0]
    conv_rows = KCONV - 1
    rim_rows = passed_along(signal[row_count - conv_rows :], "ctx", 1)
    padded = jnp.concatenate([rim_rows, signal], axis=0).astype(jnp.float32)
    preact = conv_shift
    for offset in range(KCONV):
        preact = preact + conv_taps[offset] * padded[offset : offset + row_count]
    inner_act = jax.nn.silu(preact)
    step_size = jax.nn.softplus(unscaled_step.astype(jnp.float32))
    decay_rate = -jnp.exp(log_rates)
    b_proj = proj_in[:, :NSTATE].astype(jnp.float32)
    c_proj = proj_in[:, NSTATE:].astype(jnp.float32)
    gating_f = gating.astype(jnp.float32)
    gate_act = jax.nn.silu(gating_f)
    out_grad = mamba_grad.astype(jnp.float32)
    out_drive = out_grad * gate_act
    moved_in = step_size * inner_act
    b_flat = b_proj.reshape(-1)
    c_flat = c_proj.reshape(-1)
    dt_r = lanes_view(step_size)
    u_r = lanes_view(moved_in)
    gy_r = lanes_view(out_drive)
    a_r = lanes_view(decay_rate)
    state_end, adjoint_end = mamba_summary(b_flat, c_flat, dt_r, u_r, gy_r, a_r)
    step_total = jnp.sum(dt_r, axis=0, keepdims=True)
    state_in = ctx_scan(step_total, state_end, a_r, "ctx", False)
    adjoint_in = ctx_scan(step_total, adjoint_end, a_r, "ctx", True)
    y_ssm, moved_grad, step_ssm, rate_grad_r, c_fold, b_fold = mamba_full(
        b_flat, c_flat, dt_r, u_r, gy_r, a_r, state_in, adjoint_in
    )
    mixed_out = flat_view(y_ssm) + direct_gain * inner_act
    step_grad = flat_view(step_ssm) + flat_view(moved_grad) * inner_act
    inner_grad = flat_view(moved_grad) * step_size + direct_gain * out_drive
    rate_grad = flat_view(rate_grad_r)
    b_grad = jnp.sum(b_fold, axis=(0, 3))
    c_grad = jnp.sum(c_fold, axis=(0, 3))
    skip_grad = jnp.sum(out_drive * inner_act, axis=0)
    mamba_out = (mixed_out * gate_act).astype(jnp.bfloat16)
    gating_grad = out_grad * mixed_out * silu_slope(gating_f)
    raw_grad = step_grad * jax.nn.sigmoid(unscaled_step.astype(jnp.float32))
    pre_grad = inner_grad * silu_slope(preact)
    rim_after = passed_along(shortened(pre_grad[:conv_rows]), "ctx", -1)
    extended = jnp.concatenate([pre_grad, rim_after], axis=0)
    signal_grad = jnp.zeros_like(pre_grad)
    for offset in range(KCONV):
        signal_grad = (
            signal_grad
            + conv_taps[offset] * extended[conv_rows - offset : conv_rows - offset + row_count]
        )
    tap_grad = jnp.stack(
        [jnp.sum(pre_grad * padded[offset : offset + row_count], axis=0) for offset in range(KCONV)]
    )
    bias_grad = jnp.sum(pre_grad, axis=0)
    log_grad = rate_grad * decay_rate
    weight_parts = jnp.concatenate(
        [tap_grad, bias_grad[None], log_grad, skip_grad[None]], axis=0
    )
    mix_out = jnp.stack([signal_grad, gating_grad, raw_grad]).astype(jnp.bfloat16)
    return mamba_out, mix_out, b_grad, c_grad, weight_parts


def body(
    queries,
    keys_values,
    mix_in,
    proj_bc,
    attn_cot,
    mamba_cot,
    conv_weight,
    conv_bias,
    a_log,
    skip_gain,
):
    query_in, pair_in, proj_in = shifted((queries[0], keys_values[0], proj_bc[0]), "section", 1)
    attn_grad = shifted(attn_cot[0], "section", -1)
    mix_local, cot_local, _, _, _ = lax.optimization_barrier(
        (mix_in[0], mamba_cot[0], query_in, pair_in, attn_grad)
    )
    channels = mix_local.shape[-1]
    pieces = 1
    width = channels // pieces
    arrived = []
    for piece in range(pieces):
        mix_part = mix_local[:, :, piece * width : (piece + 1) * width]
        cot_part = cot_local[:, piece * width : (piece + 1) * width]
        if arrived:
            mix_part, cot_part, _, _ = lax.optimization_barrier(
                (mix_part, cot_part) + arrived[-1]
            )
        arrived.append((shifted(mix_part, "section", 1), shifted(cot_part, "section", -1)))
    row_count = query_in.shape[0]
    first_row = (lax.axis_index("ctx") * row_count).astype(jnp.int32)
    pairs_whole = lax.all_gather(pair_in, "ctx", axis=0, tiled=True)
    seq_length = pairs_whole.shape[0]
    attn_out, query_out, pair_grad = attention(first_row, query_in, pairs_whole, attn_grad)
    whole_term = pair_grad
    first_mix, first_cot, attn_out, query_out, whole_term = lax.optimization_barrier(
        arrived[0] + (attn_out, query_out, whole_term)
    )
    arrived[0] = (first_mix, first_cot)
    key_sum = lax.psum_scatter(whole_term, "ctx", scatter_dimension=0, tiled=True)
    pair_out = key_sum
    results = []
    for piece, (mix_part, cot_part) in enumerate(arrived):
        cut = slice(piece * width, (piece + 1) * width)
        results.append(
            mamba_chunk(
                mix_part,
                cot_part,
                proj_in,
                conv_weight[0][:, cut],
                conv_bias[0][cut],
                a_log[0][:, cut],
                skip_gain[0][cut],
            )
        )
    mamba_out = jnp.concatenate([r[0] for r in results], axis=1)
    mix_out = jnp.concatenate([r[1] for r in results], axis=2)
    b_grad = sum(r[2] for r in results)
    c_grad = sum(r[3] for r in results)
    weight_parts = jnp.concatenate([r[4] for r in results], axis=1)
    weight_sum = ctx_total(weight_parts, "ctx")
    taps = conv_weight.shape[1]
    states = a_log.shape[1]
    tap_sum = weight_sum[:taps]
    bias_sum = weight_sum[taps]
    log_sum = weight_sum[taps + 1 : taps + 1 + states]
    skip_sum = weight_sum[taps + 1 + states]
    proj_out = jnp.concatenate([b_grad, c_grad], axis=1).astype(jnp.bfloat16)
    return (
        attn_out[None],
        mamba_out[None],
        query_out[None],
        pair_out[None],
        mix_out[None],
        proj_out[None],
        tap_sum[None],
        bias_sum[None],
        log_sum[None],
        skip_sum[None],
    )


def solution(mesh):
    placed = (
        P("section", "ctx", None),
        P("section", "ctx", None),
        P("section", None, "ctx", None),
        P("section", "ctx", None),
        P("section", "ctx", None),
        P("section", "ctx", None),
        P("section", None, None),
        P("section", None),
        P("section", None, None),
        P("section", None),
    )
    return jax.shard_map(
        body,
        mesh=mesh,
        in_specs=placed,
        out_specs=(
            P("section", "ctx", None),
            P("section", "ctx", None),
            P("section", "ctx", None),
            P("section", "ctx", None),
            P("section", None, "ctx", None),
            P("section", "ctx", None),
            P("section", None, None),
            P("section", None),
            P("section", None, None),
            P("section", None),
        ),
        check_vma=False,
    )
```

```python
import jax
import jax.numpy as jnp
from jax import lax
from jax.sharding import PartitionSpec as P
from jax.experimental import pallas as pl
from jax.experimental.pallas import tpu as pltpu

C = 4096
NSTATE = 8
KCONV = 4
HEADS = 16
KVHEADS = 4
HDIM = 128


def shifted(block, axis, distance):
    devices = range(lax.axis_size(axis))
    route = [((i - distance) % len(devices), i) for i in devices]
    return lax.ppermute(block, axis, route)


def passed_along(shard, axis, by):
    devices = lax.axis_size(axis)
    pairs = [(i, i + by) for i in range(devices) if 0 <= i + by < devices]
    return lax.ppermute(shard, axis, pairs)


def shortened(shard):

    def short(part):
        return part.astype(jnp.bfloat16) if part.dtype == jnp.float32 else part

    return jax.tree.map(short, shard)


def silu_slope(value):
    sigmoid_v = jax.nn.sigmoid(value)
    return sigmoid_v * (1.0 + value * (1.0 - sigmoid_v))


def attention_kernel(row_ref, q_ref, kv_ref, g_ref, o_ref, dq_ref, dkv_ref):
    rows = q_ref.shape[0]
    seq = kv_ref.shape[0]
    width = HDIM
    groups = kv_ref.shape[1] // (2 * width)
    heads = q_ref.shape[1] // width // groups
    scale = width ** (-0.5)
    query_pos = row_ref[0] + lax.broadcasted_iota(jnp.int32, (rows, seq), 0)
    key_pos = lax.broadcasted_iota(jnp.int32, (rows, seq), 1)
    allowed = key_pos <= query_pos

    def group(g, carry):
        key_col = pl.multiple_of(g * width, width)
        value_col = pl.multiple_of((groups + g) * width, width)
        keys = kv_ref[:, pl.ds(key_col, width)]
        values = kv_ref[:, pl.ds(value_col, width)]
        key_acc = jnp.zeros((seq, width), jnp.float32)
        value_acc = jnp.zeros((seq, width), jnp.float32)
        for r in range(heads):
            col = pl.multiple_of((g * heads + r) * width, width)
            cols = pl.ds(col, width)
            query = q_ref[:, cols]
            grad = g_ref[:, cols]
            scores = lax.dot_general(
                query, keys, (((1,), (1,)), ((), ())), preferred_element_type=jnp.float32
            ) * scale
            masked = jnp.where(allowed, scores, -jnp.inf)
            peak = jnp.max(masked, axis=-1, keepdims=True)
            total = jnp.sum(jnp.exp(masked - peak), axis=-1, keepdims=True)
            probs = jnp.exp(masked - (peak + jnp.log(total))).astype(jnp.bfloat16)
            output = jnp.dot(probs, values, preferred_element_type=jnp.float32).astype(
                jnp.bfloat16
            )
            o_ref[:, cols] = output
            slope = lax.dot_general(
                grad, values, (((1,), (1,)), ((), ())), preferred_element_type=jnp.float32
            )
            delta = jnp.sum(
                grad.astype(jnp.float32) * output.astype(jnp.float32), axis=-1, keepdims=True
            )
            score_grad = (probs.astype(jnp.float32) * (slope - delta)).astype(jnp.bfloat16)
            dq_ref[:, cols] = (
                jnp.dot(score_grad, keys, preferred_element_type=jnp.float32) * scale
            ).astype(jnp.bfloat16)
            key_acc = key_acc + lax.dot_general(
                score_grad, query, (((0,), (0,)), ((), ())), preferred_element_type=jnp.float32
            )
            value_acc = value_acc + lax.dot_general(
                probs, grad, (((0,), (0,)), ((), ())), preferred_element_type=jnp.float32
            )
        dkv_ref[:, pl.ds(key_col, width)] = (key_acc * scale).astype(jnp.bfloat16)
        dkv_ref[:, pl.ds(value_col, width)] = value_acc.astype(jnp.bfloat16)
        return carry

    lax.fori_loop(0, groups, group, 0)


def attention(first_row, query_in, pairs_whole, attn_grad):
    rows = query_in.shape[0]
    seq = pairs_whole.shape[0]
    smem = pl.BlockSpec(memory_space=pltpu.SMEM)
    whole = pl.BlockSpec(memory_space=pltpu.VMEM)
    flops = 12 * rows * seq * query_in.shape[1]
    return pl.pallas_call(
        attention_kernel,
        in_specs=[smem, whole, whole, whole],
        out_specs=[whole, whole, whole],
        out_shape=[
            jax.ShapeDtypeStruct(query_in.shape, jnp.bfloat16),
            jax.ShapeDtypeStruct(query_in.shape, jnp.bfloat16),
            jax.ShapeDtypeStruct(pairs_whole.shape, jnp.bfloat16),
        ],
        cost_estimate=pl.CostEstimate(
            flops=flops,
            transcendentals=2 * rows * seq * query_in.shape[1] // HDIM,
            bytes_accessed=2 * (4 * query_in.size + 2 * pairs_whole.size),
        ),
    )(first_row.reshape(1), query_in, pairs_whole, attn_grad)


LANES = 128
ROWS = 8


def fold_rows(parts):
    rows = lax.broadcasted_iota(jnp.int32, parts[0].shape, 0)

    def pair(first, second, k):
        low = (rows & k) == 0
        kept = jnp.where(low, first, second)
        moved = jnp.where(low, second, first)
        if k == 4:
            swapped = pltpu.roll(moved, 4, 0)
        else:
            swapped = jnp.where(low, pltpu.roll(moved, ROWS - k, 0), pltpu.roll(moved, k, 0))
        return kept + swapped

    stage = [pair(parts[n], parts[n + 4], 4) for n in range(4)]
    stage = [pair(stage[n], stage[n + 2], 2) for n in range(2)]
    return pair(stage[0], stage[1], 1)


def summary_kernel(b_ref, c_ref, dt_ref, u_ref, gy_ref, a_ref, s_ref, g_ref):
    steps = dt_ref.shape[0]
    count = a_ref.shape[0]
    rates = [a_ref[n] for n in range(count)]

    def advance(t, carry):
        state, decay, adjoint = carry
        dt = dt_ref[t]
        moved = u_ref[t]
        drive = gy_ref[t]
        next_state, next_decay, next_adjoint = [], [], []
        for n in range(count):
            factor = jnp.exp(dt * rates[n])
            next_state.append(factor * state[n] + b_ref[t * count + n] * moved)
            d = decay[n] * factor
            next_decay.append(d)
            next_adjoint.append(adjoint[n] + (c_ref[t * count + n] * d) * drive)
        return (tuple(next_state), tuple(next_decay), tuple(next_adjoint))

    zeros = tuple(jnp.zeros_like(r) for r in rates)
    ones = tuple(jnp.ones_like(r) for r in rates)
    state, _, adjoint = lax.fori_loop(0, steps, advance, (zeros, ones, zeros), unroll=2)
    for n in range(count):
        s_ref[n] = state[n]
        g_ref[n] = adjoint[n]


def full_kernel(
    b_ref, c_ref, dt_ref, u_ref, gy_ref, a_ref, hin_ref, gin_ref,
    y_ref, gu_ref, gdt_ref, ga_ref, gc_ref, gb_ref, hist_ref,
):
    steps = dt_ref.shape[0]
    count = a_ref.shape[0]
    rates = [a_ref[n] for n in range(count)]
    start = tuple(hin_ref[n] for n in range(count))
    for n in range(count):
        hist_ref[0, n] = start[n]

    def forward(t, state):
        dt = dt_ref[t]
        moved = u_ref[t]
        drive = gy_ref[t]
        mixed = None
        parts = []
        next_state = []
        for n in range(count):
            factor = jnp.exp(dt * rates[n])
            h = factor * state[n] + b_ref[t * count + n] * moved
            hist_ref[t + 1, n] = h
            term = c_ref[t * count + n] * h
            mixed = term if mixed is None else mixed + term
            parts.append(h * drive)
            next_state.append(h)
        y_ref[t] = mixed
        gc_ref[t] = fold_rows(parts)
        return tuple(next_state)

    lax.fori_loop(0, steps, forward, start, unroll=2)

    def backward(i, carry):
        t = steps - 1 - i
        pending, rate_acc = carry
        dt = dt_ref[t]
        moved = u_ref[t]
        drive = gy_ref[t]
        step_acc = None
        moved_acc = None
        parts = []
        next_pending = []
        next_rate = []
        for n in range(count):
            factor = jnp.exp(dt * rates[n])
            adj = c_ref[t * count + n] * drive + pending[n]
            through = adj * factor * hist_ref[t, n]
            x1 = through * rates[n]
            step_acc = x1 if step_acc is None else step_acc + x1
            next_rate.append(rate_acc[n] + through * dt)
            x2 = b_ref[t * count + n] * adj
            moved_acc = x2 if moved_acc is None else moved_acc + x2
            parts.append(adj * moved)
            next_pending.append(factor * adj)
        gdt_ref[t] = step_acc
        gu_ref[t] = moved_acc
        gb_ref[t] = fold_rows(parts)
        return (tuple(next_pending), tuple(next_rate))

    pending0 = tuple(gin_ref[n] for n in range(count))
    zeros = tuple(jnp.zeros_like(r) for r in rates)
    _, rate_acc = lax.fori_loop(0, steps, backward, (pending0, zeros), unroll=2)
    for n in range(count):
        ga_ref[n] = rate_acc[n]


def scan_specs(steps, count, blocks):
    smem = pl.BlockSpec(memory_space=pltpu.SMEM)
    rows = pl.BlockSpec((steps, ROWS, LANES), lambda j: (0, j, 0))
    states = pl.BlockSpec((count, ROWS, LANES), lambda j: (0, j, 0))
    return smem, rows, states


def mamba_summary(b_flat, c_flat, dt_r, u_r, gy_r, a_r):
    steps = dt_r.shape[0]
    count = a_r.shape[0]
    blocks = dt_r.shape[1] // ROWS
    smem, rows, states = scan_specs(steps, count, blocks)
    shape = jax.ShapeDtypeStruct(a_r.shape, jnp.float32)
    elems = steps * count * dt_r.shape[1] * LANES
    return pl.pallas_call(
        summary_kernel,
        grid=(blocks,),
        in_specs=[smem, smem, rows, rows, rows, states],
        out_specs=[states, states],
        out_shape=[shape, shape],
        cost_estimate=pl.CostEstimate(
            flops=9 * elems, transcendentals=elems, bytes_accessed=4 * 3 * dt_r.size
        ),
    )(b_flat, c_flat, dt_r, u_r, gy_r, a_r)


def mamba_full(b_flat, c_flat, dt_r, u_r, gy_r, a_r, h_in, g_in):
    steps = dt_r.shape[0]
    count = a_r.shape[0]
    blocks = dt_r.shape[1] // ROWS
    smem, rows, states = scan_specs(steps, count, blocks)
    folded = pl.BlockSpec((None, steps, count, LANES), lambda j: (j, 0, 0, 0))
    row_shape = jax.ShapeDtypeStruct(dt_r.shape, jnp.float32)
    fold_shape = jax.ShapeDtypeStruct((blocks, steps, count, LANES), jnp.float32)
    elems = steps * count * dt_r.shape[1] * LANES
    return pl.pallas_call(
        full_kernel,
        grid=(blocks,),
        in_specs=[smem, smem, rows, rows, rows, states, states, states],
        out_specs=[rows, rows, rows, states, folded, folded],
        out_shape=[
            row_shape,
            row_shape,
            row_shape,
            jax.ShapeDtypeStruct(a_r.shape, jnp.float32),
            fold_shape,
            fold_shape,
        ],
        scratch_shapes=[pltpu.VMEM((steps + 1, count, ROWS, LANES), jnp.float32)],
        cost_estimate=pl.CostEstimate(
            flops=30 * elems, transcendentals=2 * elems, bytes_accessed=4 * 6 * dt_r.size
        ),
    )(b_flat, c_flat, dt_r, u_r, gy_r, a_r, h_in, g_in)


def lanes_view(matrix):
    return matrix.reshape(matrix.shape[0], matrix.shape[1] // LANES, LANES)


def flat_view(stacked):
    return stacked.reshape(stacked.shape[0], stacked.shape[1] * stacked.shape[2])


def ctx_total(parts, axis):
    count = lax.axis_size(axis)
    if count & (count - 1):
        return jnp.sum(lax.all_gather(parts, axis), axis=0)
    distance = 1
    while distance < count:
        pairs = [(i, i ^ distance) for i in range(count)]
        parts = parts + lax.ppermute(parts, axis, pairs)
        distance *= 2
    return parts


def mamba_chunk(mixture, mamba_grad, proj_in, conv_taps, conv_shift, log_rates, direct_gain, fence):
    signal = mixture[0]
    gating = mixture[1]
    unscaled_step = mixture[2]
    row_count = signal.shape[0]
    conv_rows = KCONV - 1
    rim_rows = passed_along(signal[row_count - conv_rows :], "ctx", 1)
    padded = jnp.concatenate([rim_rows, signal], axis=0).astype(jnp.float32)
    preact = conv_shift
    for offset in range(KCONV):
        preact = preact + conv_taps[offset] * padded[offset : offset + row_count]
    inner_act = jax.nn.silu(preact)
    step_size = jax.nn.softplus(unscaled_step.astype(jnp.float32))
    decay_rate = -jnp.exp(log_rates)
    b_proj = proj_in[:, :NSTATE].astype(jnp.float32)
    c_proj = proj_in[:, NSTATE:].astype(jnp.float32)
    gating_f = gating.astype(jnp.float32)
    gate_act = jax.nn.silu(gating_f)
    out_grad = mamba_grad.astype(jnp.float32)
    out_drive = out_grad * gate_act
    moved_in = step_size * inner_act
    b_flat = b_proj.reshape(-1)
    c_flat = c_proj.reshape(-1)
    dt_r = lanes_view(step_size)
    u_r = lanes_view(moved_in)
    gy_r = lanes_view(out_drive)
    a_r = lanes_view(decay_rate)
    state_end, adjoint_end = mamba_summary(b_flat, c_flat, dt_r, u_r, gy_r, a_r)
    step_total = jnp.sum(dt_r, axis=0)
    own_decay = jnp.exp(a_r * step_total[None])
    gathered = lax.all_gather(
        jnp.concatenate([state_end, adjoint_end, own_decay], axis=0).astype(jnp.bfloat16), "ctx"
    ).astype(jnp.float32)
    gathered, fence = lax.optimization_barrier((gathered, fence))
    fence = lax.psum_scatter(fence, "ctx", scatter_dimension=0, tiled=True)
    count = a_r.shape[0]
    place = lax.axis_index("ctx")
    devices = gathered.shape[0]
    state_in = jnp.zeros_like(state_end)
    adjoint_in = jnp.zeros_like(adjoint_end)
    for other in range(devices):
        decay = gathered[other, 2 * count :]
        state_in = jnp.where(
            other < place, decay * state_in + gathered[other, :count], state_in
        )
    for other in reversed(range(devices)):
        decay = gathered[other, 2 * count :]
        adjoint_in = jnp.where(
            other > place, decay * adjoint_in + gathered[other, count : 2 * count], adjoint_in
        )
    y_ssm, moved_grad, step_ssm, rate_grad_r, c_fold, b_fold = mamba_full(
        b_flat, c_flat, dt_r, u_r, gy_r, a_r, state_in, adjoint_in
    )
    y_ssm, moved_grad, step_ssm, fence = lax.optimization_barrier(
        (y_ssm, moved_grad, step_ssm, fence)
    )
    mixed_out = flat_view(y_ssm) + direct_gain * inner_act
    step_grad = flat_view(step_ssm) + flat_view(moved_grad) * inner_act
    inner_grad = flat_view(moved_grad) * step_size + direct_gain * out_drive
    rate_grad = flat_view(rate_grad_r)
    b_grad = jnp.sum(b_fold, axis=(0, 3))
    c_grad = jnp.sum(c_fold, axis=(0, 3))
    skip_grad = jnp.sum(out_drive * inner_act, axis=0)
    mamba_out = (mixed_out * gate_act).astype(jnp.bfloat16)
    gating_grad = out_grad * mixed_out * silu_slope(gating_f)
    raw_grad = step_grad * jax.nn.sigmoid(unscaled_step.astype(jnp.float32))
    pre_grad = inner_grad * silu_slope(preact)
    rim_after = passed_along(shortened(pre_grad[:conv_rows]), "ctx", -1)
    extended = jnp.concatenate([pre_grad, rim_after], axis=0)
    signal_grad = jnp.zeros_like(pre_grad)
    for offset in range(KCONV):
        signal_grad = (
            signal_grad
            + conv_taps[offset] * extended[conv_rows - offset : conv_rows - offset + row_count]
        )
    tap_grad = jnp.stack(
        [jnp.sum(pre_grad * padded[offset : offset + row_count], axis=0) for offset in range(KCONV)]
    )
    bias_grad = jnp.sum(pre_grad, axis=0)
    log_grad = rate_grad * decay_rate
    weight_parts = jnp.concatenate(
        [tap_grad, bias_grad[None], log_grad, skip_grad[None]], axis=0
    )
    mix_out = jnp.stack([signal_grad, gating_grad, raw_grad]).astype(jnp.bfloat16)
    return mamba_out, mix_out, b_grad, c_grad, weight_parts, fence


def body(
    queries,
    keys_values,
    mix_in,
    proj_bc,
    attn_cot,
    mamba_cot,
    conv_weight,
    conv_bias,
    a_log,
    skip_gain,
):
    query_in, pair_in, proj_in = shifted((queries[0], keys_values[0], proj_bc[0]), "section", 1)
    attn_grad = shifted(attn_cot[0], "section", -1)
    mix_local, cot_local, _, _, _ = lax.optimization_barrier(
        (mix_in[0], mamba_cot[0], query_in, pair_in, attn_grad)
    )
    channels = mix_local.shape[-1]
    pieces = 1
    width = channels // pieces
    arrived = []
    for piece in range(pieces):
        mix_part = mix_local[:, :, piece * width : (piece + 1) * width]
        cot_part = cot_local[:, piece * width : (piece + 1) * width]
        if arrived:
            mix_part, cot_part, _, _ = lax.optimization_barrier(
                (mix_part, cot_part) + arrived[-1]
            )
        arrived.append((shifted(mix_part, "section", 1), shifted(cot_part, "section", -1)))
    row_count = query_in.shape[0]
    first_row = (lax.axis_index("ctx") * row_count).astype(jnp.int32)
    pairs_whole = lax.all_gather(pair_in, "ctx", axis=0, tiled=True)
    seq_length = pairs_whole.shape[0]
    attn_out, query_out, pair_grad = attention(first_row, query_in, pairs_whole, attn_grad)
    whole_term = pair_grad
    first_mix, first_cot, attn_out, query_out, whole_term = lax.optimization_barrier(
        arrived[0] + (attn_out, query_out, whole_term)
    )
    arrived[0] = (first_mix, first_cot)
    pair_out = whole_term
    results = []
    for piece, (mix_part, cot_part) in enumerate(arrived):
        cut = slice(piece * width, (piece + 1) * width)
        results.append(
            mamba_chunk(
                mix_part,
                cot_part,
                proj_in,
                conv_weight[0][:, cut],
                conv_bias[0][cut],
                a_log[0][:, cut],
                skip_gain[0][cut],
                pair_out,
            )
        )
        pair_out = results[-1][5]
    mamba_out = jnp.concatenate([r[0] for r in results], axis=1)
    mix_out = jnp.concatenate([r[1] for r in results], axis=2)
    b_grad = sum(r[2] for r in results)
    c_grad = sum(r[3] for r in results)
    weight_parts = jnp.concatenate([r[4] for r in results], axis=1)
    spare = max(0, 17 - weight_parts.shape[0])
    padded_parts = jnp.pad(weight_parts, ((0, spare), (0, 0))).astype(jnp.bfloat16)
    weight_sum = jnp.sum(lax.all_gather(padded_parts, "ctx").astype(jnp.float32), axis=0)
    taps = conv_weight.shape[1]
    states = a_log.shape[1]
    tap_sum = weight_sum[:taps]
    bias_sum = weight_sum[taps]
    log_sum = weight_sum[taps + 1 : taps + 1 + states]
    skip_sum = weight_sum[taps + 1 + states]
    proj_out = jnp.concatenate([b_grad, c_grad], axis=1).astype(jnp.bfloat16)
    return (
        attn_out[None],
        mamba_out[None],
        query_out[None],
        pair_out[None],
        mix_out[None],
        proj_out[None],
        tap_sum[None],
        bias_sum[None],
        log_sum[None],
        skip_sum[None],
    )


def solution(mesh):
    placed = (
        P("section", "ctx", None),
        P("section", "ctx", None),
        P("section", None, "ctx", None),
        P("section", "ctx", None),
        P("section", "ctx", None),
        P("section", "ctx", None),
        P("section", None, None),
        P("section", None),
        P("section", None, None),
        P("section", None),
    )
    return jax.shard_map(
        body,
        mesh=mesh,
        in_specs=placed,
        out_specs=(
            P("section", "ctx", None),
            P("section", "ctx", None),
            P("section", "ctx", None),
            P("section", "ctx", None),
            P("section", None, "ctx", None),
            P("section", "ctx", None),
            P("section", None, None),
            P("section", None),
            P("section", None, None),
            P("section", None),
        ),
        check_vma=False,
    )
```
